256 devices in a mesh: src: 16 (over y, x), tgt: 16 (over z, core).
Axes of the slice: x: 4, y: 4, z: 8, core: 2. Of those that a mesh axis runs over, the one named last changes fastest.
Arguments:
- src_emb_t: bfloat16 [300, 16384], P(None, 'src'), may hold values from -6 to 6
- tgt_emb_t: bfloat16 [300, 32768], P(None, 'tgt'), may hold values from -6 to 6
- core: float32 [300, 300], replicated, may hold values from -0.08 to 0.2
- src_logw: float32 [16384], P('src'), may hold values from -1.5 to 1.5
- tgt_logw: float32 [32768], P('tgt'), may hold values from -1.5 to 1.5
Outputs:
- src_potential: float32 [16384], P('src')
- tgt_potential: float32 [32768], P('tgt')
- next_core: float32 [300, 300], replicated
The draws below stay inside these ranges and needn't reach their ends.
All inputs are finite; a program needn't handle non-finite values.
Results may differ from the reference program's by a relative error of at most 0.0036.
Values sent between devices are 32-bit elements; how exact they have to be, the bound alone decides.
No kernel may reach another device: no remote copies, remote signals or barrier semaphores. Data moves between devices by JAX's collectives and lax.ppermute only.
A program may use at most 64 MiB of HBM per device.

```python
import jax
import jax.numpy as jnp
from jax import lax

D = 300
ROWS = 1024
ITERS = 3
NS = 16384
NT = 32768
N_SRC = 16


def embed_pair(key):
    base = jax.random.fold_in(key, 11)
    key_src = jax.random.fold_in(base, 0)
    key_tgt = jax.random.fold_in(base, 1)
    key_cols = jax.random.fold_in(base, 3)
    source = jnp.clip(1.0 + jax.random.normal(key_src, (D, NS), jnp.float32), -6.0, 6.0)
    target = jnp.clip(jax.random.normal(key_tgt, (D, NT), jnp.float32), -6.0, 6.0)
    shunned = jax.random.randint(key_cols, (4,), 0, NT - 8)
    column_index = jnp.arange(NT)[None, :]
    hit = jnp.any(column_index[:, :, None] == shunned[None, None, :], axis=2)
    target = jnp.where(hit, -6.0, target).astype(jnp.float32)
    return (source, target)


def draw_src_emb_t(key, part):
    source, target = embed_pair(key)
    return source.astype(jnp.bfloat16)


def draw_tgt_emb_t(key, part):
    source, target = embed_pair(key)
    return target.astype(jnp.bfloat16)


def draw_core(key, part):
    inner = jax.random.fold_in(key, 5)
    noise = jnp.clip(jax.random.normal(inner, (D, D), jnp.float32), -4.0, 4.0)
    return (noise + 6.0 * jnp.eye(D, dtype=jnp.float32)) * (6.0 / D)


def level_of(key, shape, cuts, smallest, top_value):
    def one(dim, shards_of):
        draws = jax.random.uniform(jax.random.fold_in(jax.random.fold_in(key, 6), dim), (shards_of,), jnp.float32, smallest / len(cuts), top_value / len(cuts))
        return jnp.repeat(jnp.exp(draws), shape[dim] // shards_of).reshape((-1,) + (1,) * (len(shape) - dim - 1))

    loudness = one(*cuts[0])
    for cut in cuts[1:]:
        loudness = loudness * one(*cut)
    return loudness


def setup_inputs(seed: int = 0) -> dict:
    streams_of = jax.random.split(jax.random.key(seed), 6)
    src_emb_t = draw_src_emb_t(jax.random.fold_in(streams_of[5], 71), 0)
    tgt_emb_t = draw_tgt_emb_t(jax.random.fold_in(streams_of[5], 71), 0)
    core = draw_core(jax.random.fold_in(streams_of[5], 71), 0)
    src_logw = jnp.clip(jax.random.uniform(streams_of[3], (NS,), jnp.float32, -1.5, 1.5) * level_of(streams_of[3], (NS,), ((0, 16),), -0.4, 0.0), -1.5, 1.5)
    tgt_logw = jnp.clip(jax.random.uniform(streams_of[4], (NT,), jnp.float32, -1.5, 1.5) * level_of(streams_of[4], (NT,), ((0, 16),), -0.4, 0.0), -1.5, 1.5)
    return dict(src_emb_t=src_emb_t, tgt_emb_t=tgt_emb_t, core=core, src_logw=src_logw, tgt_logw=tgt_logw)


def reference(src_emb_t, tgt_emb_t, core, src_logw, tgt_logw):
    projected = jnp.dot(core.T, src_emb_t.astype(jnp.float32), precision=lax.Precision.HIGHEST).astype(jnp.bfloat16)
    proj_blocks = projected.reshape(D, N_SRC, ROWS).transpose(1, 0, 2)
    emb_blocks = src_emb_t.reshape(D, N_SRC, ROWS).transpose(1, 0, 2)
    logw_blocks = src_logw.reshape(N_SRC, ROWS)

    def scores_of(block):
        return lax.dot_general(block, tgt_emb_t, (((0,), (0,)), ((), ())), preferred_element_type=jnp.float32)

    tgt_pot = jnp.zeros((NT,), jnp.float32)
    src_pot = jnp.zeros((NS,), jnp.float32)
    for step in range(ITERS):
        def row_step(inputs):
            block, logw = inputs
            shifted = scores_of(block) + tgt_pot[None, :]
            peaks = jnp.max(shifted, axis=1)
            totals = jnp.sum(jnp.exp(shifted - peaks[:, None]), axis=1)
            return logw - (peaks + jnp.log(totals))

        src_pot = lax.map(row_step, (proj_blocks, logw_blocks)).reshape(NS)
        pot_blocks = src_pot.reshape(N_SRC, ROWS)

        def col_step(carry, inputs):
            peaks, totals = carry
            block, pot = inputs
            shifted = scores_of(block) + pot[:, None]
            newpeak = jnp.maximum(peaks, jnp.max(shifted, axis=0))
            totals = totals * jnp.exp(peaks - newpeak) + jnp.sum(jnp.exp(shifted - newpeak[None, :]), axis=0)
            return (newpeak, totals), None

        start = (jnp.full((NT,), -1e30, jnp.float32), jnp.zeros((NT,), jnp.float32))
        (peaks, totals), unused = lax.scan(col_step, start, (proj_blocks, pot_blocks))
        tgt_pot = tgt_logw - (peaks + jnp.log(totals))

    pot_blocks = src_pot.reshape(N_SRC, ROWS)

    def core_step(acc, inputs):
        block, emb, pot = inputs
        plan = jnp.exp(scores_of(block) + pot[:, None] + tgt_pot[None, :]).astype(jnp.bfloat16)
        panel = lax.dot_general(plan, tgt_emb_t, (((1,), (1,)), ((), ())), preferred_element_type=jnp.float32)
        return acc + jnp.dot(emb.astype(jnp.float32), panel, precision=lax.Precision.HIGHEST), None

    acc, unused = lax.scan(core_step, jnp.zeros((D, D), jnp.float32), (proj_blocks, emb_blocks, pot_blocks))
    next_core = acc * (D / NS)
    return src_pot, tgt_pot, next_core
```

```python
import jax
import jax.numpy as jnp
from jax import lax
from jax.sharding import PartitionSpec as P

D = 300
ITERS = 3


def merge_lse(peaks, totals, axis):
    n = lax.axis_size(axis)
    pair = jnp.stack([peaks, totals])
    sent = jnp.broadcast_to(pair[None], (n,) + pair.shape)
    got = lax.all_to_all(sent, axis, 0, 0, tiled=False)
    top = jnp.max(got[:, 0], axis=0)
    total = jnp.sum(got[:, 1] * jnp.exp(got[:, 0] - top[None]), axis=0)
    return top + jnp.log(total)


def row_lse(shifted):
    peaks = jnp.max(shifted, axis=1)
    totals = jnp.sum(jnp.exp(shifted - peaks[:, None]), axis=1)
    return merge_lse(peaks, totals, "tgt")


def col_lse(shifted):
    peaks = jnp.max(shifted, axis=0)
    totals = jnp.sum(jnp.exp(shifted - peaks[None, :]), axis=0)
    return merge_lse(peaks, totals, "src")


def butterfly_sum(x, axis):
    n = lax.axis_size(axis)
    d = 1
    while d < n:
        x = x + lax.ppermute(x, axis, [(i, i ^ d) for i in range(n)])
        d *= 2
    return x


def sum_all(c):
    n = lax.axis_size("tgt")
    rows = c.shape[0]
    padded = -(-rows // n) * n
    x = jnp.pad(c, ((0, padded - rows), (0, 0)))
    idx = lax.axis_index("tgt")
    d = n // 2
    while d >= 1:
        half = x.shape[0] // 2
        lo, hi = x[:half], x[half:]
        upper = (idx // d) % 2 == 1
        send = jnp.where(upper, lo, hi)
        keep = jnp.where(upper, hi, lo)
        x = keep + lax.ppermute(send, "tgt", [(i, i ^ d) for i in range(n)])
        d //= 2
    x = butterfly_sum(x, "src")
    d = 1
    while d < n:
        upper = (idx // d) % 2 == 1
        other = lax.ppermute(x, "tgt", [(i, i ^ d) for i in range(n)])
        x = jnp.where(upper, jnp.concatenate([other, x]), jnp.concatenate([x, other]))
        d *= 2
    return x[:rows]


def per_device(src_emb_t, tgt_emb_t, core, src_logw, tgt_logw):
    projected = jnp.dot(
        core.T, src_emb_t.astype(jnp.float32), precision=lax.Precision.HIGHEST
    ).astype(jnp.bfloat16)
    scores = lax.dot_general(
        projected, tgt_emb_t, (((0,), (0,)), ((), ())), preferred_element_type=jnp.float32
    )
    tgt_pot = jnp.zeros((tgt_emb_t.shape[1],), jnp.float32)
    src_pot = jnp.zeros((src_emb_t.shape[1],), jnp.float32)
    for step in range(ITERS):
        src_pot = src_logw - row_lse(scores + tgt_pot[None, :])
        tgt_pot = tgt_logw - col_lse(scores + src_pot[:, None])
    plan = jnp.exp(scores + src_pot[:, None] + tgt_pot[None, :]).astype(jnp.bfloat16)
    total_words = src_emb_t.shape[1] * lax.axis_size("src")
    panel = lax.dot_general(
        plan, tgt_emb_t, (((1,), (1,)), ((), ())), preferred_element_type=jnp.float32
    )
    partial_core = jnp.dot(src_emb_t.astype(jnp.float32), panel, precision=lax.Precision.HIGHEST)
    next_core = sum_all(partial_core) * (D / total_words)
    return (src_pot, tgt_pot, next_core)


def solution(mesh):
    placed = (P(None, "src"), P(None, "tgt"), P(), P("src"), P("tgt"))
    return jax.shard_map(
        per_device, mesh=mesh, in_specs=placed, out_specs=(P("src"), P("tgt"), P()), check_vma=False
    )
```

```python
import jax
import jax.numpy as jnp
from jax import lax
from jax.sharding import PartitionSpec as P

D = 300
ITERS = 3


def merge_lse(peaks, totals, axis):
    n = lax.axis_size(axis)
    pair = jnp.stack([peaks, totals])
    sent = jnp.broadcast_to(pair[None], (n,) + pair.shape)
    got = lax.all_to_all(sent, axis, 0, 0, tiled=False)
    top = jnp.max(got[:, 0], axis=0)
    total = jnp.sum(got[:, 1] * jnp.exp(got[:, 0] - top[None]), axis=0)
    return top + jnp.log(total)


def row_lse(shifted):
    peaks = jnp.max(shifted, axis=1)
    totals = jnp.sum(jnp.exp(shifted - peaks[:, None]), axis=1)
    return merge_lse(peaks, totals, "tgt")


def col_lse(shifted):
    peaks = jnp.max(shifted, axis=0)
    totals = jnp.sum(jnp.exp(shifted - peaks[None, :]), axis=0)
    return merge_lse(peaks, totals, "src")


def butterfly_sum(x, axis):
    n = lax.axis_size(axis)
    d = 1
    while d < n:
        x = x + lax.ppermute(x, axis, [(i, i ^ d) for i in range(n)])
        d *= 2
    return x


def sum_all(c):
    axes = ("src", "tgt")
    n = lax.axis_size(axes)
    rows, cols = c.shape
    k = rows * cols
    per = -(-k // n)
    x = jnp.pad(c.reshape(-1), (0, per * n - k)).reshape(n, per)
    x = jnp.sum(lax.all_to_all(x, axes, 0, 0, tiled=False), axis=0)
    x = lax.all_to_all(jnp.broadcast_to(x[None], (n, per)), axes, 0, 0, tiled=False).reshape(-1)[:k]
    return x.reshape(rows, cols)


def per_device(src_emb_t, tgt_emb_t, core, src_logw, tgt_logw):
    projected = jnp.dot(
        core.T, src_emb_t.astype(jnp.float32), precision=lax.Precision.HIGHEST
    ).astype(jnp.bfloat16)
    scores = lax.dot_general(
        projected, tgt_emb_t, (((0,), (0,)), ((), ())), preferred_element_type=jnp.float32
    )
    tgt_pot = jnp.zeros((tgt_emb_t.shape[1],), jnp.float32)
    src_pot = jnp.zeros((src_emb_t.shape[1],), jnp.float32)
    for step in range(ITERS):
        src_pot = src_logw - row_lse(scores + tgt_pot[None, :])
        tgt_pot = tgt_logw - col_lse(scores + src_pot[:, None])
    plan = jnp.exp(scores + src_pot[:, None] + tgt_pot[None, :]).astype(jnp.bfloat16)
    total_words = src_emb_t.shape[1] * lax.axis_size("src")
    panel = lax.dot_general(
        plan, tgt_emb_t, (((1,), (1,)), ((), ())), preferred_element_type=jnp.float32
    )
    partial_core = jnp.dot(src_emb_t.astype(jnp.float32), panel, precision=lax.Precision.HIGHEST)
    next_core = sum_all(partial_core) * (D / total_words)
    return (src_pot, tgt_pot, next_core)


def solution(mesh):
    placed = (P(None, "src"), P(None, "tgt"), P(), P("src"), P("tgt"))
    return jax.shard_map(
        per_device, mesh=mesh, in_specs=placed, out_specs=(P("src"), P("tgt"), P()), check_vma=False
    )
```

```python
import jax
import jax.numpy as jnp
from jax import lax
from jax.sharding import PartitionSpec as P

D = 300
ITERS = 3


def merge_lse(peaks, totals, axis):
    n = lax.axis_size(axis)
    pair = jnp.stack([peaks, totals])
    sent = jnp.broadcast_to(pair[None], (n,) + pair.shape)
    got = lax.all_to_all(sent, axis, 0, 0, tiled=False)
    top = jnp.max(got[:, 0], axis=0)
    total = jnp.sum(got[:, 1] * jnp.exp(got[:, 0] - top[None]), axis=0)
    return top + jnp.log(total)


def row_lse(shifted):
    peaks = jnp.max(shifted, axis=1)
    totals = jnp.sum(jnp.exp(shifted - peaks[:, None]), axis=1)
    return merge_lse(peaks, totals, "tgt")


def col_lse(shifted):
    peaks = jnp.max(shifted, axis=0)
    totals = jnp.sum(jnp.exp(shifted - peaks[None, :]), axis=0)
    return merge_lse(peaks, totals, "src")


def butterfly_sum(x, axis):
    n = lax.axis_size(axis)
    d = 1
    while d < n:
        x = x + lax.ppermute(x, axis, [(i, i ^ d) for i in range(n)])
        d *= 2
    return x


def sum_all(c, scale):
    n = lax.axis_size("tgt")
    m = lax.axis_size("src")
    rows, cols = c.shape
    k = rows * cols
    per = -(-k // n)
    x = jnp.pad(c.reshape(-1), (0, per * n - k)).reshape(n, per)
    x = jnp.sum(lax.all_to_all(x, "tgt", 0, 0, tiled=True), axis=0)
    x = jnp.sum(lax.all_to_all(jnp.broadcast_to(x[None], (m, per)), "src", 0, 0, tiled=True), axis=0) * scale
    x = lax.all_to_all(jnp.broadcast_to(x[None], (n, per)), "tgt", 0, 0, tiled=True)
    return x.reshape(-1)[:k].reshape(rows, cols)


def per_device(src_emb_t, tgt_emb_t, core, src_logw, tgt_logw):
    projected = jnp.dot(
        core.T, src_emb_t.astype(jnp.float32), precision=lax.Precision.HIGHEST
    ).astype(jnp.bfloat16)
    scores = lax.dot_general(
        projected, tgt_emb_t, (((0,), (0,)), ((), ())), preferred_element_type=jnp.float32
    )
    tgt_pot = jnp.zeros((tgt_emb_t.shape[1],), jnp.float32)
    src_pot = jnp.zeros((src_emb_t.shape[1],), jnp.float32)
    for step in range(ITERS):
        src_pot = src_logw - row_lse(scores + tgt_pot[None, :])
        tgt_pot = tgt_logw - col_lse(scores + src_pot[:, None])
    plan = jnp.exp(scores + src_pot[:, None] + tgt_pot[None, :]).astype(jnp.bfloat16)
    total_words = src_emb_t.shape[1] * lax.axis_size("src")
    panel = lax.dot_general(
        plan, tgt_emb_t, (((1,), (1,)), ((), ())), preferred_element_type=jnp.float32
    )
    partial_core = jnp.dot(src_emb_t.astype(jnp.float32), panel, precision=lax.Precision.HIGHEST)
    next_core = sum_all(partial_core, D / total_words)
    return (src_pot, tgt_pot, next_core)


def solution(mesh):
    placed = (P(None, "src"), P(None, "tgt"), P(), P("src"), P("tgt"))
    return jax.shard_map(
        per_device, mesh=mesh, in_specs=placed, out_specs=(P("src"), P("tgt"), P()), check_vma=False
    )
```

```python
import jax
import jax.numpy as jnp
from jax import lax
from jax.sharding import PartitionSpec as P

D = 300
ITERS = 3


def merge_lse(peaks, totals, axis):
    n = lax.axis_size(axis)
    pair = jnp.stack([peaks, totals])
    sent = jnp.broadcast_to(pair[None], (n,) + pair.shape)
    got = lax.all_to_all(sent, axis, 0, 0, tiled=False)
    top = jnp.max(got[:, 0], axis=0)
    total = jnp.sum(got[:, 1] * jnp.exp(got[:, 0] - top[None]), axis=0)
    return top + jnp.log(total)


def row_lse(shifted):
    peaks = jnp.max(shifted, axis=1)
    totals = jnp.sum(jnp.exp(shifted - peaks[:, None]), axis=1)
    return merge_lse(peaks, totals, "tgt")


def col_lse(shifted):
    peaks = jnp.max(shifted, axis=0)
    totals = jnp.sum(jnp.exp(shifted - peaks[None, :]), axis=0)
    return merge_lse(peaks, totals, "src")


def butterfly_sum(x, axis):
    n = lax.axis_size(axis)
    d = 1
    while d < n:
        x = x + lax.ppermute(x, axis, [(i, i ^ d) for i in range(n)])
        d *= 2
    return x


def sum_all(c, scale):
    n = lax.axis_size("src")
    m = lax.axis_size("tgt")
    rows, cols = c.shape
    k = rows * cols
    per = -(-k // n)
    x = jnp.pad(c.reshape(-1), (0, per * n - k)).reshape(n, per)
    x = jnp.sum(lax.all_to_all(x, "src", 0, 0, tiled=True), axis=0)
    x = jnp.sum(lax.all_to_all(jnp.broadcast_to(x[None], (m, per)), "tgt", 0, 0, tiled=True), axis=0) * scale
    x = lax.all_to_all(jnp.broadcast_to(x[None], (n, per)), "src", 0, 0, tiled=True)
    return x.reshape(-1)[:k].reshape(rows, cols)


def per_device(src_emb_t, tgt_emb_t, core, src_logw, tgt_logw):
    projected = jnp.dot(
        core.T, src_emb_t.astype(jnp.float32), precision=lax.Precision.HIGHEST
    ).astype(jnp.bfloat16)
    scores = lax.dot_general(
        projected, tgt_emb_t, (((0,), (0,)), ((), ())), preferred_element_type=jnp.float32
    )
    tgt_pot = jnp.zeros((tgt_emb_t.shape[1],), jnp.float32)
    src_pot = jnp.zeros((src_emb_t.shape[1],), jnp.float32)
    for step in range(ITERS):
        src_pot = src_logw - row_lse(scores + tgt_pot[None, :])
        tgt_pot = tgt_logw - col_lse(scores + src_pot[:, None])
    plan = jnp.exp(scores + src_pot[:, None] + tgt_pot[None, :]).astype(jnp.bfloat16)
    total_words = src_emb_t.shape[1] * lax.axis_size("src")
    panel = lax.dot_general(
        plan, tgt_emb_t, (((1,), (1,)), ((), ())), preferred_element_type=jnp.float32
    )
    partial_core = jnp.dot(src_emb_t.astype(jnp.float32), panel, precision=lax.Precision.HIGHEST)
    next_core = sum_all(partial_core, D / total_words)
    return (src_pot, tgt_pot, next_core)


def solution(mesh):
    placed = (P(None, "src"), P(None, "tgt"), P(), P("src"), P("tgt"))
    return jax.shard_map(
        per_device, mesh=mesh, in_specs=placed, out_specs=(P("src"), P("tgt"), P()), check_vma=False
    )
```

```python
import jax
import jax.numpy as jnp
from jax import lax
from jax.sharding import Mesh, PartitionSpec as P

D = 300
ITERS = 3
TGT = ("tz", "tc")
WIDE = ("src", "tc")


def merge_lse(peaks, totals, axis):
    n = lax.axis_size(axis)
    pair = jnp.stack([peaks, totals])
    sent = jnp.broadcast_to(pair[None], (n,) + pair.shape)
    got = lax.all_to_all(sent, axis, 0, 0, tiled=False)
    top = jnp.max(got[:, 0], axis=0)
    total = jnp.sum(got[:, 1] * jnp.exp(got[:, 0] - top[None]), axis=0)
    return top + jnp.log(total)


def row_lse(shifted):
    peaks = jnp.max(shifted, axis=1)
    totals = jnp.sum(jnp.exp(shifted - peaks[:, None]), axis=1)
    return merge_lse(peaks, totals, TGT)


def col_lse(shifted):
    peaks = jnp.max(shifted, axis=0)
    totals = jnp.sum(jnp.exp(shifted - peaks[None, :]), axis=0)
    return merge_lse(peaks, totals, "src")


def butterfly_sum(x, axis):
    n = lax.axis_size(axis)
    d = 1
    while d < n:
        x = x + lax.ppermute(x, axis, [(i, i ^ d) for i in range(n)])
        d *= 2
    return x


def sum_all(c, scale):
    n = lax.axis_size(WIDE)
    m = lax.axis_size("tz")
    rows, cols = c.shape
    k = rows * cols
    per = -(-k // n)
    x = jnp.pad(c.reshape(-1), (0, per * n - k)).reshape(n, per)
    x = jnp.sum(lax.all_to_all(x, WIDE, 0, 0, tiled=True), axis=0)
    x = jnp.sum(lax.all_to_all(jnp.broadcast_to(x[None], (m, per)), "tz", 0, 0, tiled=True), axis=0) * scale
    x = lax.all_to_all(jnp.broadcast_to(x[None], (n, per)), WIDE, 0, 0, tiled=True)
    return x.reshape(-1)[:k].reshape(rows, cols)


def per_device(src_emb_t, tgt_emb_t, core, src_logw, tgt_logw):
    projected = jnp.dot(
        core.T, src_emb_t.astype(jnp.float32), precision=lax.Precision.HIGHEST
    ).astype(jnp.bfloat16)
    scores = lax.dot_general(
        projected, tgt_emb_t, (((0,), (0,)), ((), ())), preferred_element_type=jnp.float32
    )
    tgt_pot = jnp.zeros((tgt_emb_t.shape[1],), jnp.float32)
    src_pot = jnp.zeros((src_emb_t.shape[1],), jnp.float32)
    for step in range(ITERS):
        src_pot = src_logw - row_lse(scores + tgt_pot[None, :])
        tgt_pot = tgt_logw - col_lse(scores + src_pot[:, None])
    plan = jnp.exp(scores + src_pot[:, None] + tgt_pot[None, :]).astype(jnp.bfloat16)
    total_words = src_emb_t.shape[1] * lax.axis_size("src")
    panel = lax.dot_general(
        plan, tgt_emb_t, (((1,), (1,)), ((), ())), preferred_element_type=jnp.float32
    )
    partial_core = jnp.dot(src_emb_t.astype(jnp.float32), panel, precision=lax.Precision.HIGHEST)
    next_core = sum_all(partial_core, D / total_words)
    return (src_pot, tgt_pot, next_core)


def solution(mesh):
    n_src, n_tgt = mesh.devices.shape
    fine = Mesh(mesh.devices.reshape(n_src, n_tgt // 2, 2), ("src",) + TGT)
    placed = (P(None, "src"), P(None, TGT), P(), P("src"), P(TGT))
    return jax.shard_map(
        per_device, mesh=fine, in_specs=placed, out_specs=(P("src"), P(TGT), P()), check_vma=False
    )
```

```python
import jax
import jax.numpy as jnp
from jax import lax
from jax.sharding import Mesh, PartitionSpec as P

D = 300
ITERS = 3
TGT = ("tz", "tc")
WIDE = ("src", "tc")


def merge_lse(peaks, totals, axis):
    n = lax.axis_size(axis)
    pair = jnp.stack([peaks, totals])
    sent = jnp.broadcast_to(pair[None], (n,) + pair.shape)
    got = lax.all_to_all(sent, axis, 0, 0, tiled=False)
    top = jnp.max(got[:, 0], axis=0)
    total = jnp.sum(got[:, 1] * jnp.exp(got[:, 0] - top[None]), axis=0)
    return top + jnp.log(total)


def row_lse(shifted):
    peaks = jnp.max(shifted, axis=1)
    totals = jnp.sum(jnp.exp(shifted - peaks[:, None]), axis=1)
    return merge_lse(peaks, totals, ("tc", "tz"))


def col_lse(shifted):
    peaks = jnp.max(shifted, axis=0)
    totals = jnp.sum(jnp.exp(shifted - peaks[None, :]), axis=0)
    return merge_lse(peaks, totals, "src")


def butterfly_sum(x, axis):
    n = lax.axis_size(axis)
    d = 1
    while d < n:
        x = x + lax.ppermute(x, axis, [(i, i ^ d) for i in range(n)])
        d *= 2
    return x


def sum_all(c, scale):
    n = lax.axis_size(WIDE)
    m = lax.axis_size("tz")
    rows, cols = c.shape
    k = rows * cols
    per = -(-k // n)
    x = jnp.pad(c.reshape(-1), (0, per * n - k)).reshape(n, per)
    x = jnp.sum(lax.all_to_all(x, WIDE, 0, 0, tiled=True), axis=0)
    x = jnp.sum(lax.all_to_all(jnp.broadcast_to(x[None], (m, per)), "tz", 0, 0, tiled=True), axis=0) * scale
    x = lax.all_to_all(jnp.broadcast_to(x[None], (n, per)), WIDE, 0, 0, tiled=True)
    return x.reshape(-1)[:k].reshape(rows, cols)


def per_device(src_emb_t, tgt_emb_t, core, src_logw, tgt_logw):
    projected = jnp.dot(
        core.T, src_emb_t.astype(jnp.float32), precision=lax.Precision.HIGHEST
    ).astype(jnp.bfloat16)
    scores = lax.dot_general(
        projected, tgt_emb_t, (((0,), (0,)), ((), ())), preferred_element_type=jnp.float32
    )
    tgt_pot = jnp.zeros((tgt_emb_t.shape[1],), jnp.float32)
    src_pot = jnp.zeros((src_emb_t.shape[1],), jnp.float32)
    for step in range(ITERS):
        src_pot = src_logw - row_lse(scores + tgt_pot[None, :])
        tgt_pot = tgt_logw - col_lse(scores + src_pot[:, None])
    plan = jnp.exp(scores + src_pot[:, None] + tgt_pot[None, :]).astype(jnp.bfloat16)
    total_words = src_emb_t.shape[1] * lax.axis_size("src")
    panel = lax.dot_general(
        plan, tgt_emb_t, (((1,), (1,)), ((), ())), preferred_element_type=jnp.float32
    )
    partial_core = jnp.dot(src_emb_t.astype(jnp.float32), panel, precision=lax.Precision.HIGHEST)
    next_core = sum_all(partial_core, D / total_words)
    return (src_pot, tgt_pot, next_core)


def solution(mesh):
    n_src, n_tgt = mesh.devices.shape
    fine = Mesh(mesh.devices.reshape(n_src, n_tgt // 2, 2), ("src",) + TGT)
    placed = (P(None, "src"), P(None, TGT), P(), P("src"), P(TGT))
    return jax.shard_map(
        per_device, mesh=fine, in_specs=placed, out_specs=(P("src"), P(TGT), P()), check_vma=False
    )
```

```python
import jax
import jax.numpy as jnp
from jax import lax
from jax.sharding import Mesh, PartitionSpec as P

D = 300
ITERS = 3
TGT = ("tzh", "tzl", "tc")
Z = ("tzl", "tzh")
WIDE = ("tc", "src")


def merge_lse(peaks, totals, axis):
    n = lax.axis_size(axis)
    pair = jnp.stack([peaks, totals])
    sent = jnp.broadcast_to(pair[None], (n,) + pair.shape)
    got = lax.all_to_all(sent, axis, 0, 0, tiled=False)
    top = jnp.max(got[:, 0], axis=0)
    total = jnp.sum(got[:, 1] * jnp.exp(got[:, 0] - top[None]), axis=0)
    return top + jnp.log(total)


def row_lse(shifted):
    peaks = jnp.max(shifted, axis=1)
    totals = jnp.sum(jnp.exp(shifted - peaks[:, None]), axis=1)
    return merge_lse(peaks, totals, ("tc", "tzh", "tzl"))


def col_lse(shifted):
    peaks = jnp.max(shifted, axis=0)
    totals = jnp.sum(jnp.exp(shifted - peaks[None, :]), axis=0)
    return merge_lse(peaks, totals, "src")


def butterfly_sum(x, axis):
    n = lax.axis_size(axis)
    d = 1
    while d < n:
        x = x + lax.ppermute(x, axis, [(i, i ^ d) for i in range(n)])
        d *= 2
    return x


def sum_all(c, scale):
    n = lax.axis_size(WIDE)
    m = lax.axis_size(Z)
    rows, cols = c.shape
    k = rows * cols
    per = -(-k // n)
    x = jnp.pad(c.reshape(-1), (0, per * n - k)).reshape(n, per)
    x = jnp.sum(lax.all_to_all(x, WIDE, 0, 0, tiled=True), axis=0)
    x = jnp.sum(lax.all_to_all(jnp.broadcast_to(x[None], (m, per)), Z, 0, 0, tiled=True), axis=0) * scale
    x = lax.all_to_all(jnp.broadcast_to(x[None], (n, per)), WIDE, 0, 0, tiled=True)
    return x.reshape(-1)[:k].reshape(rows, cols)


def per_device(src_emb_t, tgt_emb_t, core, src_logw, tgt_logw):
    projected = jnp.dot(
        core.T, src_emb_t.astype(jnp.float32), precision=lax.Precision.HIGHEST
    ).astype(jnp.bfloat16)
    scores = lax.dot_general(
        projected, tgt_emb_t, (((0,), (0,)), ((), ())), preferred_element_type=jnp.float32
    )
    tgt_pot = jnp.zeros((tgt_emb_t.shape[1],), jnp.float32)
    src_pot = jnp.zeros((src_emb_t.shape[1],), jnp.float32)
    for step in range(ITERS):
        src_pot = src_logw - row_lse(scores + tgt_pot[None, :])
        tgt_pot = tgt_logw - col_lse(scores + src_pot[:, None])
    plan = jnp.exp(scores + src_pot[:, None] + tgt_pot[None, :]).astype(jnp.bfloat16)
    total_words = src_emb_t.shape[1] * lax.axis_size("src")
    panel = lax.dot_general(
        plan, tgt_emb_t, (((1,), (1,)), ((), ())), preferred_element_type=jnp.float32
    )
    partial_core = jnp.dot(src_emb_t.astype(jnp.float32), panel, precision=lax.Precision.HIGHEST)
    next_core = sum_all(partial_core, D / total_words)
    return (src_pot, tgt_pot, next_core)


def solution(mesh):
    n_src, n_tgt = mesh.devices.shape
    fine = Mesh(mesh.devices.reshape(n_src, n_tgt // 4, 2, 2), ("src",) + TGT)
    placed = (P(None, "src"), P(None, TGT), P(), P("src"), P(TGT))
    return jax.shard_map(
        per_device, mesh=fine, in_specs=placed, out_specs=(P("src"), P(TGT), P()), check_vma=False
    )
```

```python
import jax
import jax.numpy as jnp
from jax import lax
from jax.sharding import Mesh, PartitionSpec as P

D = 300
ITERS = 3
TGT = ("tzh", "tzl", "tc")
Z = ("tzl", "tzh")
WIDE = ("tc", "src")


def merge_lse(peaks, totals, axes):
    for axis in axes:
        n = lax.axis_size(axis)
        pair = jnp.stack([peaks, totals])
        if n == 2:
            other = lax.ppermute(pair, axis, [(0, 1), (1, 0)])
            top = jnp.maximum(peaks, other[0])
            totals = totals * jnp.exp(peaks - top) + other[1] * jnp.exp(other[0] - top)
            peaks = top
        else:
            got = lax.all_to_all(jnp.broadcast_to(pair[None], (n,) + pair.shape), axis, 0, 0, tiled=False)
            peaks = jnp.max(got[:, 0], axis=0)
            totals = jnp.sum(got[:, 1] * jnp.exp(got[:, 0] - peaks[None]), axis=0)
    return peaks + jnp.log(totals)


def row_lse(shifted):
    peaks = jnp.max(shifted, axis=1)
    totals = jnp.sum(jnp.exp(shifted - peaks[:, None]), axis=1)
    return merge_lse(peaks, totals, ("tc", ("tzl", "tzh")))


def col_lse(shifted):
    peaks = jnp.max(shifted, axis=0)
    totals = jnp.sum(jnp.exp(shifted - peaks[None, :]), axis=0)
    return merge_lse(peaks, totals, ("src",))


def butterfly_sum(x, axis):
    n = lax.axis_size(axis)
    d = 1
    while d < n:
        x = x + lax.ppermute(x, axis, [(i, i ^ d) for i in range(n)])
        d *= 2
    return x


def sum_all(c, scale):
    n = lax.axis_size(WIDE)
    m = lax.axis_size(Z)
    rows, cols = c.shape
    k = rows * cols
    per = -(-k // n)
    x = jnp.pad(c.reshape(-1), (0, per * n - k)).reshape(n, per)
    x = jnp.sum(lax.all_to_all(x, WIDE, 0, 0, tiled=True), axis=0)
    x = jnp.sum(lax.all_to_all(jnp.broadcast_to(x[None], (m, per)), Z, 0, 0, tiled=True), axis=0) * scale
    x = lax.all_to_all(jnp.broadcast_to(x[None], (n, per)), WIDE, 0, 0, tiled=True)
    return x.reshape(-1)[:k].reshape(rows, cols)


def per_device(src_emb_t, tgt_emb_t, core, src_logw, tgt_logw):
    projected = jnp.dot(
        core.T, src_emb_t.astype(jnp.float32), precision=lax.Precision.HIGHEST
    ).astype(jnp.bfloat16)
    scores = lax.dot_general(
        projected, tgt_emb_t, (((0,), (0,)), ((), ())), preferred_element_type=jnp.float32
    )
    tgt_pot = jnp.zeros((tgt_emb_t.shape[1],), jnp.float32)
    src_pot = jnp.zeros((src_emb_t.shape[1],), jnp.float32)
    for step in range(ITERS):
        src_pot = src_logw - row_lse(scores + tgt_pot[None, :])
        tgt_pot = tgt_logw - col_lse(scores + src_pot[:, None])
    plan = jnp.exp(scores + src_pot[:, None] + tgt_pot[None, :]).astype(jnp.bfloat16)
    total_words = src_emb_t.shape[1] * lax.axis_size("src")
    panel = lax.dot_general(
        plan, tgt_emb_t, (((1,), (1,)), ((), ())), preferred_element_type=jnp.float32
    )
    partial_core = jnp.dot(src_emb_t.astype(jnp.float32), panel, precision=lax.Precision.HIGHEST)
    next_core = sum_all(partial_core, D / total_words)
    return (src_pot, tgt_pot, next_core)


def solution(mesh):
    n_src, n_tgt = mesh.devices.shape
    fine = Mesh(mesh.devices.reshape(n_src, n_tgt // 4, 2, 2), ("src",) + TGT)
    placed = (P(None, "src"), P(None, TGT), P(), P("src"), P(TGT))
    return jax.shard_map(
        per_device, mesh=fine, in_specs=placed, out_specs=(P("src"), P(TGT), P()), check_vma=False
    )
```
